256 devices in a mesh: section: 4 (over x), dp: 32 (over z, y), mp: 2 (over core).
Axes of the slice: x: 4, y: 4, z: 8, core: 2. Of those that a mesh axis runs over, the one named last changes fastest.
Arguments:
- frames: bfloat16 [8192, 2560], P('dp', 'mp'), may hold values from -6 to 6
- frame_count: int32 [32], P('dp'), may hold values from 64 to 256, as said below
- norm_gain: float32 [4, 2560], P('section'), may hold values from 0.5 to 1.5
- weight_in: bfloat16 [4, 2560, 5120], P('section', 'dp', 'mp'), may hold values from -0.125 to 0.125
- weight_out: bfloat16 [4, 5120, 2560], P('section', 'mp', 'dp'), may hold values from -0.15625 to 0.15625
Outputs:
- states: bfloat16 [4, 8192, 2560], P('section', 'dp', 'mp')
The draws below stay inside these ranges and needn't reach their ends.
Inputs may be any that keep to these rules, and one draw needn't show every extreme that they name: `frame_count`: each entry lies between 64 and 256; one entry equals 256 in every draw.
All inputs are finite; a program needn't handle non-finite values.
Results may differ from the reference program's by a relative error of at most 0.017.
Values may be sent and summed in bfloat16 or wider, within the bound.
No kernel may reach another device: no remote copies, remote signals or barrier semaphores. Data moves between devices by JAX's collectives and lax.ppermute only.
A program may use at most 128 MiB of HBM per device.

```python
import jax
import jax.numpy as jnp
from jax import lax

D = 2560
FFW = 5120
TOK_DEV = 256
LAYERS = 4
TOKENS = 8192
N_DP = 32
N_MP = 2


def draw_frame_count(key, part):
    lowest = TOK_DEV // 4
    counts = jax.random.randint(jax.random.fold_in(key, 11), (N_DP,), lowest, TOK_DEV + 1)
    fullest = jax.random.randint(jax.random.fold_in(key, 12), (), 0, N_DP)
    return jnp.where(jnp.arange(N_DP) == fullest, TOK_DEV, counts).astype(jnp.int32)


def raised(result, own_key, source, target, blocks, factor):
    owner, partner = [(jnp.arange(result.shape[position]) // (result.shape[position] // blocks)).reshape([-1 if axis == position else 1 for axis in range(result.ndim)]) for position in (source, target)]
    chosen = jax.random.permutation(own_key, blocks)[partner]
    strong = (owner == chosen) | (owner == (partner + blocks // 2) % blocks)
    return jnp.where(strong, factor * result, result)


def block_levels(own_key, dims, shards, low, top_value):
    level = 1.0
    for dim, shards_of in shards:
        heights = jax.random.uniform(jax.random.fold_in(jax.random.fold_in(own_key, 6), dim), (shards_of,), jnp.float32, low / len(shards), top_value / len(shards))
        level = level * jnp.repeat(jnp.exp(heights), dims[dim] // shards_of).reshape((-1,) + (1,) * (len(dims) - 1 - dim))
    return level


def bell_draw(own_key, shape, scale, limit, split=(), kind=jnp.bfloat16):
    values = jax.random.normal(own_key, shape, jnp.float32) * scale
    if len(split) > 0:
        values = block_levels(own_key, shape, split, -0.22, 0.18) * values
    return jnp.clip(values, min=-limit, max=limit).astype(kind)


def gaussian_with(key, shape, width, reach, split, heavy, kind=jnp.bfloat16):
    drawn = width * jax.random.normal(key, shape, jnp.float32)
    if split:
        drawn = drawn * block_levels(key, shape, split, -0.22, 0.18)
    return jnp.clip(raised(drawn, jax.random.fold_in(key, 3), *heavy), -reach, reach).astype(kind)


def setup_inputs(seed: int = 0) -> dict:
    key_list = jax.random.split(jax.random.key(seed), 6)
    return {
        "frames": bell_draw(key_list[0], (TOKENS, D), 1.0, 6.0, ((0, 32), (1, 2))),
        "frame_count": draw_frame_count(jax.random.fold_in(key_list[5], 71), 0),
        "norm_gain": jnp.clip(1.0 + 0.1 * jax.random.normal(key_list[2], (LAYERS, D), jnp.float32), 0.5, 1.5),
        "weight_in": bell_draw(key_list[3], (LAYERS, D, FFW), D ** -0.5, 0.125, ((0, 4), (1, 32), (2, 2))),
        "weight_out": gaussian_with(key_list[4], (LAYERS, FFW, D), FFW ** -0.5, 0.15625, ((0, 4), (1, 2), (2, 32)), (1, 2, 32, 2.75)),
    }


def apply_block(values, gain, matrix_in, matrix_out):
    wide = values.astype(jnp.float32)
    meansq = lax.optimization_barrier(jnp.mean(wide * wide, axis=-1, keepdims=True))
    normed = (wide * lax.rsqrt(meansq + 1e-06) * gain).astype(jnp.bfloat16)
    hidden = jax.nn.gelu(jnp.dot(normed, matrix_in, preferred_element_type=jnp.float32), approximate=False).astype(jnp.bfloat16)
    group = FFW // N_MP
    summed = jnp.zeros(wide.shape, jnp.float32)
    for index in range(N_MP):
        partial_term = jnp.dot(hidden[:, index * group:(index + 1) * group], matrix_out[index * group:(index + 1) * group], preferred_element_type=jnp.float32).astype(jnp.bfloat16)
        partial_term = lax.optimization_barrier(partial_term)
        summed = summed + partial_term.astype(jnp.float32)
    return (wide + summed).astype(jnp.bfloat16)

def reference(frames, frame_count, norm_gain, weight_in, weight_out):
    row_ids = jnp.arange(TOKENS, dtype=jnp.int32)
    limits = frame_count[row_ids // TOK_DEV]
    live = row_ids % TOK_DEV < limits
    current = jnp.where(live[:, None], frames, jnp.zeros_like(frames))
    outputs = []
    for layer in range(LAYERS):
        current = apply_block(current, norm_gain[layer], weight_in[layer], weight_out[layer])
        outputs.append(current)
    return jnp.stack(outputs, axis=0)
```

```python
import jax
import jax.numpy as jnp
from jax import lax
from jax.sharding import PartitionSpec as P


def passed_along(value, axis, steps):
    count = lax.axis_size(axis)
    first, last = (max(0, -steps), min(count, count - steps))
    return lax.ppermute(value, axis, [(source, source + steps) for source in range(first, last)])


def per_device(frames, frame_count, norm_gain, weight_in, weight_out):
    segment_count = lax.axis_size("section")
    segment_index = lax.axis_index("section")
    half_index = lax.axis_index("mp")
    matrix_in = lax.all_gather(weight_in[0], "dp", axis=0, tiled=True)
    matrix_out_t = lax.all_gather(weight_out[0].T, "dp", axis=0, tiled=True)
    gain_row = norm_gain[0]
    local_rows, width_local = frames.shape
    live_count = frame_count[0]
    row_ids = jnp.arange(local_rows, dtype=jnp.int32)
    first = jnp.where((row_ids < live_count)[:, None], frames, jnp.zeros_like(frames))

    def apply_layer(current):
        whole = lax.all_gather(current, "mp", axis=1, tiled=True)
        wide = whole.astype(jnp.float32)
        meansq = jnp.mean(wide * wide, axis=-1, keepdims=True)
        normed = (wide * lax.rsqrt(meansq + 1e-06) * gain_row).astype(jnp.bfloat16)
        hidden = jax.nn.gelu(
            jnp.dot(normed, matrix_in, preferred_element_type=jnp.float32), approximate=False
        ).astype(jnp.bfloat16)
        partial_term = lax.dot_general(
            hidden, matrix_out_t, (((1,), (1,)), ((), ())), preferred_element_type=jnp.float32
        ).astype(jnp.bfloat16)
        halves = partial_term.reshape(local_rows, 2, width_local)
        keep = jnp.where(half_index == 0, halves[:, 0], halves[:, 1])
        send = jnp.where(half_index == 0, halves[:, 1], halves[:, 0])
        other = lax.ppermute(send, "mp", [(0, 1), (1, 0)])
        summed = keep.astype(jnp.float32) + other.astype(jnp.float32)
        return (current.astype(jnp.float32) + summed).astype(jnp.bfloat16)

    def advance(moment, carry):
        current, stored = carry
        result = apply_layer(current)
        stored = jnp.where(segment_index == moment, result, stored)
        return (passed_along(result, "section", 1), stored)

    initial = (first, jnp.zeros((local_rows, width_local), jnp.bfloat16))
    leftover, stored = lax.fori_loop(0, segment_count, advance, initial)
    return stored.reshape(1, local_rows, width_local)


def solution(mesh):
    in_specs = (
        P("dp", "mp"),
        P("dp"),
        P("section", None),
        P("section", "dp", "mp"),
        P("section", "mp", "dp"),
    )
    out_specs = P("section", "dp", "mp")
    return jax.shard_map(
        per_device, mesh=mesh, in_specs=in_specs, out_specs=out_specs, check_vma=False
    )
```

```python
import jax
import jax.numpy as jnp
from jax import lax
from jax.sharding import PartitionSpec as P


def passed_along(value, axis, steps):
    count = lax.axis_size(axis)
    first, last = (max(0, -steps), min(count, count - steps))
    return lax.ppermute(value, axis, [(source, source + steps) for source in range(first, last)])


def per_device(frames, frame_count, norm_gain, weight_in, weight_out):
    segment_count = lax.axis_size("section")
    segment_index = lax.axis_index("section")
    half_index = lax.axis_index("mp")
    matrix_in = lax.all_gather(weight_in[0], "dp", axis=0, tiled=True)
    matrix_out_t = lax.all_gather(weight_out[0].T, "dp", axis=0, tiled=True)
    gain_row = norm_gain[0]
    local_rows, width_local = frames.shape
    live_count = frame_count[0]
    row_ids = jnp.arange(local_rows, dtype=jnp.int32)
    first = jnp.where((row_ids < live_count)[:, None], frames, jnp.zeros_like(frames))

    def apply_layer(current):
        partner = lax.ppermute(current, "mp", [(0, 1), (1, 0)])
        whole = jnp.where(
            half_index == 0,
            jnp.concatenate([current, partner], axis=1),
            jnp.concatenate([partner, current], axis=1),
        )
        wide = whole.astype(jnp.float32)
        meansq = jnp.mean(wide * wide, axis=-1, keepdims=True)
        normed = (wide * lax.rsqrt(meansq + 1e-06) * gain_row).astype(jnp.bfloat16)
        hidden = jax.nn.gelu(
            jnp.dot(normed, matrix_in, preferred_element_type=jnp.float32), approximate=False
        ).astype(jnp.bfloat16)
        partial_term = lax.dot_general(
            hidden, matrix_out_t, (((1,), (1,)), ((), ())), preferred_element_type=jnp.float32
        ).astype(jnp.bfloat16)
        keep = lax.dynamic_slice_in_dim(partial_term, half_index * width_local, width_local, axis=1)
        send = lax.dynamic_slice_in_dim(
            partial_term, (1 - half_index) * width_local, width_local, axis=1
        )
        other = lax.ppermute(send, "mp", [(0, 1), (1, 0)])
        summed = keep.astype(jnp.float32) + other.astype(jnp.float32)
        return (current.astype(jnp.float32) + summed).astype(jnp.bfloat16)

    def advance(moment, carry):
        current, stored = carry
        result = apply_layer(current)
        stored = jnp.where(segment_index == moment, result, stored)
        return (passed_along(result, "section", 1), stored)

    initial = (first, jnp.zeros((local_rows, width_local), jnp.bfloat16))
    leftover, stored = lax.fori_loop(0, segment_count, advance, initial)
    return stored.reshape(1, local_rows, width_local)


def solution(mesh):
    in_specs = (
        P("dp", "mp"),
        P("dp"),
        P("section", None),
        P("section", "dp", "mp"),
        P("section", "mp", "dp"),
    )
    out_specs = P("section", "dp", "mp")
    return jax.shard_map(
        per_device, mesh=mesh, in_specs=in_specs, out_specs=out_specs, check_vma=False
    )
```

```python
import jax
import jax.numpy as jnp
from jax import lax
from jax.sharding import PartitionSpec as P

CHUNKS = 4


def passed_along(value, axis, steps):
    count = lax.axis_size(axis)
    first, last = (max(0, -steps), min(count, count - steps))
    return lax.ppermute(value, axis, [(source, source + steps) for source in range(first, last)])


def per_device(frames, frame_count, norm_gain, weight_in, weight_out):
    segment_count = lax.axis_size("section")
    segment_index = lax.axis_index("section")
    half_index = lax.axis_index("mp")
    hidden_local = weight_in.shape[2]
    piece = hidden_local // CHUNKS
    chunks = []
    for index in range(CHUNKS):
        cols = slice(index * piece, (index + 1) * piece)
        chunk_in = lax.all_gather(weight_in[0][:, cols], "dp", axis=0, tiled=True)
        chunk_out = lax.all_gather(weight_out[0][cols, :].T, "dp", axis=0, tiled=True)
        chunks.append((chunk_in, chunk_out))
    gain_row = norm_gain[0]
    local_rows, width_local = frames.shape
    live_count = frame_count[0]
    row_ids = jnp.arange(local_rows, dtype=jnp.int32)
    first = jnp.where((row_ids < live_count)[:, None], frames, jnp.zeros_like(frames))

    def apply_layer(current):
        partner = lax.ppermute(current, "mp", [(0, 1), (1, 0)])
        whole = jnp.where(
            half_index == 0,
            jnp.concatenate([current, partner], axis=1),
            jnp.concatenate([partner, current], axis=1),
        )
        wide = whole.astype(jnp.float32)
        meansq = jnp.mean(wide * wide, axis=-1, keepdims=True)
        normed = (wide * lax.rsqrt(meansq + 1e-06) * gain_row).astype(jnp.bfloat16)
        total = None
        for chunk_in, chunk_out in chunks:
            hidden = jax.nn.gelu(
                jnp.dot(normed, chunk_in, preferred_element_type=jnp.float32), approximate=False
            ).astype(jnp.bfloat16)
            term = lax.dot_general(
                hidden, chunk_out, (((1,), (1,)), ((), ())), preferred_element_type=jnp.float32
            )
            total = term if total is None else total + term
        partial_term = total.astype(jnp.bfloat16)
        keep = lax.dynamic_slice_in_dim(partial_term, half_index * width_local, width_local, axis=1)
        send = lax.dynamic_slice_in_dim(
            partial_term, (1 - half_index) * width_local, width_local, axis=1
        )
        other = lax.ppermute(send, "mp", [(0, 1), (1, 0)])
        summed = keep.astype(jnp.float32) + other.astype(jnp.float32)
        return (current.astype(jnp.float32) + summed).astype(jnp.bfloat16)

    result = apply_layer(first)
    stored = jnp.where(segment_index == 0, result, jnp.zeros_like(result))

    def advance(moment, carry):
        previous, stored = carry
        result = apply_layer(passed_along(previous, "section", 1))
        stored = jnp.where(segment_index == moment, result, stored)
        return (result, stored)

    leftover, stored = lax.fori_loop(1, segment_count, advance, (result, stored))
    return stored.reshape(1, local_rows, width_local)


def solution(mesh):
    in_specs = (
        P("dp", "mp"),
        P("dp"),
        P("section", None),
        P("section", "dp", "mp"),
        P("section", "mp", "dp"),
    )
    out_specs = P("section", "dp", "mp")
    return jax.shard_map(
        per_device, mesh=mesh, in_specs=in_specs, out_specs=out_specs, check_vma=False
    )
```

```python
import jax
import jax.numpy as jnp
from jax import lax
from jax.sharding import PartitionSpec as P


def passed_along(value, axis, steps):
    count = lax.axis_size(axis)
    first, last = (max(0, -steps), min(count, count - steps))
    return lax.ppermute(value, axis, [(source, source + steps) for source in range(first, last)])


def per_device(frames, frame_count, norm_gain, weight_in, weight_out):
    segment_count = lax.axis_size("section")
    segment_index = lax.axis_index("section")
    half_index = lax.axis_index("mp")
    both = jnp.stack([weight_in[0], weight_out[0].T])
    gathered = lax.all_gather(both, "dp", axis=1, tiled=True)
    matrix_in = gathered[0]
    matrix_out_t = gathered[1]
    gain_row = norm_gain[0]
    local_rows, width_local = frames.shape
    live_count = frame_count[0]
    row_ids = jnp.arange(local_rows, dtype=jnp.int32)
    first = jnp.where((row_ids < live_count)[:, None], frames, jnp.zeros_like(frames))

    def apply_layer(current):
        partner = lax.ppermute(current, "mp", [(0, 1), (1, 0)])
        whole = jnp.where(
            half_index == 0,
            jnp.concatenate([current, partner], axis=1),
            jnp.concatenate([partner, current], axis=1),
        )
        wide = whole.astype(jnp.float32)
        meansq = jnp.mean(wide * wide, axis=-1, keepdims=True)
        normed = (wide * lax.rsqrt(meansq + 1e-06) * gain_row).astype(jnp.bfloat16)
        hidden = jax.nn.gelu(
            jnp.dot(normed, matrix_in, preferred_element_type=jnp.float32), approximate=False
        ).astype(jnp.bfloat16)
        partial_term = lax.dot_general(
            hidden, matrix_out_t, (((1,), (1,)), ((), ())), preferred_element_type=jnp.float32
        ).astype(jnp.bfloat16)
        keep = lax.dynamic_slice_in_dim(partial_term, half_index * width_local, width_local, axis=1)
        send = lax.dynamic_slice_in_dim(
            partial_term, (1 - half_index) * width_local, width_local, axis=1
        )
        other = lax.ppermute(send, "mp", [(0, 1), (1, 0)])
        summed = keep.astype(jnp.float32) + other.astype(jnp.float32)
        return (current.astype(jnp.float32) + summed).astype(jnp.bfloat16)

    result = apply_layer(first)
    stored = jnp.where(segment_index == 0, result, jnp.zeros_like(result))

    def advance(moment, carry):
        previous, stored = carry
        result = apply_layer(passed_along(previous, "section", 1))
        stored = jnp.where(segment_index == moment, result, stored)
        return (result, stored)

    leftover, stored = lax.fori_loop(1, segment_count, advance, (result, stored))
    return stored.reshape(1, local_rows, width_local)


def solution(mesh):
    in_specs = (
        P("dp", "mp"),
        P("dp"),
        P("section", None),
        P("section", "dp", "mp"),
        P("section", "mp", "dp"),
    )
    out_specs = P("section", "dp", "mp")
    return jax.shard_map(
        per_device, mesh=mesh, in_specs=in_specs, out_specs=out_specs, check_vma=False
    )
```

```python
import jax
import jax.numpy as jnp
from jax import lax
from jax.sharding import PartitionSpec as P


def passed_along(value, axis, steps):
    count = lax.axis_size(axis)
    first, last = (max(0, -steps), min(count, count - steps))
    return lax.ppermute(value, axis, [(source, source + steps) for source in range(first, last)])


def per_device(frames, frame_count, norm_gain, weight_in, weight_out):
    segment_count = lax.axis_size("section")
    segment_index = lax.axis_index("section")
    half_index = lax.axis_index("mp")
    both = jnp.stack([weight_in[0], weight_out[0].T])
    gathered = lax.all_gather(both, "dp", axis=1, tiled=True)
    gain_row = norm_gain[0]
    local_rows, width_local = frames.shape
    live_count = frame_count[0]
    row_ids = jnp.arange(local_rows, dtype=jnp.int32)
    first = jnp.where((row_ids < live_count)[:, None], frames, jnp.zeros_like(frames))

    def apply_layer(current):
        partner = lax.ppermute(current, "mp", [(0, 1), (1, 0)])
        whole = jnp.where(
            half_index == 0,
            jnp.concatenate([current, partner], axis=1),
            jnp.concatenate([partner, current], axis=1),
        )
        wide = whole.astype(jnp.float32)
        meansq = jnp.mean(wide * wide, axis=-1, keepdims=True)
        normed = (wide * lax.rsqrt(meansq + 1e-06) * gain_row).astype(jnp.bfloat16)
        hidden = jax.nn.gelu(
            jnp.dot(normed, gathered[0], preferred_element_type=jnp.float32), approximate=False
        ).astype(jnp.bfloat16)
        partial_term = lax.dot_general(
            hidden, gathered[1], (((1,), (1,)), ((), ())), preferred_element_type=jnp.float32
        ).astype(jnp.bfloat16)
        keep = lax.dynamic_slice_in_dim(partial_term, half_index * width_local, width_local, axis=1)
        send = lax.dynamic_slice_in_dim(
            partial_term, (1 - half_index) * width_local, width_local, axis=1
        )
        other = lax.ppermute(send, "mp", [(0, 1), (1, 0)])
        summed = keep.astype(jnp.float32) + other.astype(jnp.float32)
        return (current.astype(jnp.float32) + summed).astype(jnp.bfloat16)

    result = apply_layer(first)
    stored = jnp.where(segment_index == 0, result, jnp.zeros_like(result))

    def advance(moment, carry):
        previous, stored = carry
        result = apply_layer(passed_along(previous, "section", 1))
        stored = jnp.where(segment_index == moment, result, stored)
        return (result, stored)

    leftover, stored = lax.fori_loop(1, segment_count, advance, (result, stored))
    return stored.reshape(1, local_rows, width_local)


def solution(mesh):
    in_specs = (
        P("dp", "mp"),
        P("dp"),
        P("section", None),
        P("section", "dp", "mp"),
        P("section", "mp", "dp"),
    )
    out_specs = P("section", "dp", "mp")
    return jax.shard_map(
        per_device, mesh=mesh, in_specs=in_specs, out_specs=out_specs, check_vma=False
    )
```

```python
import jax
import jax.numpy as jnp
from jax import lax
from jax.experimental import pallas as pl
from jax.experimental.pallas import tpu as pltpu
from jax.sharding import PartitionSpec as P

TILE = 512


def ffn_body(normed_ref, win_ref, wout_ref, out_ref, acc_ref):
    step = pl.program_id(0)

    @pl.when(step == 0)
    def _():
        acc_ref[...] = jnp.zeros_like(acc_ref)

    pre = jnp.dot(normed_ref[...], win_ref[0], preferred_element_type=jnp.float32)
    hidden = (0.5 * pre * (1.0 + lax.erf(pre * 0.7071067811865476))).astype(jnp.bfloat16)
    acc_ref[...] += lax.dot_general(
        hidden, wout_ref[0], (((1,), (1,)), ((), ())), preferred_element_type=jnp.float32
    )

    @pl.when(step == pl.num_programs(0) - 1)
    def _():
        out_ref[...] = acc_ref[...].astype(out_ref.dtype)


def ffn(normed, gathered, interpret=False):
    rows, width = normed.shape
    hidden_units = gathered.shape[2]
    return pl.pallas_call(
        ffn_body,
        grid=(hidden_units // TILE,),
        in_specs=[
            pl.BlockSpec((rows, width), lambda j: (0, 0)),
            pl.BlockSpec((1, width, TILE), lambda j: (0, 0, j)),
            pl.BlockSpec((1, width, TILE), lambda j: (1, 0, j)),
        ],
        out_specs=pl.BlockSpec((rows, width), lambda j: (0, 0)),
        out_shape=jax.ShapeDtypeStruct((rows, width), jnp.bfloat16),
        scratch_shapes=[pltpu.VMEM((rows, width), jnp.float32)],
        compiler_params=pltpu.CompilerParams(vmem_limit_bytes=48 << 20),
        interpret=interpret,
    )(normed, gathered, gathered)


def passed_along(value, axis, steps):
    count = lax.axis_size(axis)
    first, last = (max(0, -steps), min(count, count - steps))
    return lax.ppermute(value, axis, [(source, source + steps) for source in range(first, last)])


def per_device(frames, frame_count, norm_gain, weight_in, weight_out):
    segment_count = lax.axis_size("section")
    segment_index = lax.axis_index("section")
    half_index = lax.axis_index("mp")
    both = jnp.stack([weight_in[0], weight_out[0].T])
    gathered = lax.all_gather(both, "dp", axis=1, tiled=True)
    gain_row = norm_gain[0]
    local_rows, width_local = frames.shape
    live_count = frame_count[0]
    row_ids = jnp.arange(local_rows, dtype=jnp.int32)
    first = jnp.where((row_ids < live_count)[:, None], frames, jnp.zeros_like(frames))

    def apply_layer(current):
        partner = lax.ppermute(current, "mp", [(0, 1), (1, 0)])
        whole = jnp.where(
            half_index == 0,
            jnp.concatenate([current, partner], axis=1),
            jnp.concatenate([partner, current], axis=1),
        )
        wide = whole.astype(jnp.float32)
        meansq = jnp.mean(wide * wide, axis=-1, keepdims=True)
        normed = (wide * lax.rsqrt(meansq + 1e-06) * gain_row).astype(jnp.bfloat16)
        partial_term = ffn(normed, gathered)
        keep = lax.dynamic_slice_in_dim(partial_term, half_index * width_local, width_local, axis=1)
        send = lax.dynamic_slice_in_dim(
            partial_term, (1 - half_index) * width_local, width_local, axis=1
        )
        other = lax.ppermute(send, "mp", [(0, 1), (1, 0)])
        summed = keep.astype(jnp.float32) + other.astype(jnp.float32)
        return (current.astype(jnp.float32) + summed).astype(jnp.bfloat16)

    result = apply_layer(first)
    stored = jnp.where(segment_index == 0, result, jnp.zeros_like(result))

    def advance(moment, carry):
        previous, stored = carry
        result = apply_layer(passed_along(previous, "section", 1))
        stored = jnp.where(segment_index == moment, result, stored)
        return (result, stored)

    leftover, stored = lax.fori_loop(1, segment_count, advance, (result, stored))
    return stored.reshape(1, local_rows, width_local)


def solution(mesh):
    in_specs = (
        P("dp", "mp"),
        P("dp"),
        P("section", None),
        P("section", "dp", "mp"),
        P("section", "mp", "dp"),
    )
    out_specs = P("section", "dp", "mp")
    return jax.shard_map(
        per_device, mesh=mesh, in_specs=in_specs, out_specs=out_specs, check_vma=False
    )
```

```python
import jax
import jax.numpy as jnp
from jax import lax
from jax.experimental import pallas as pl
from jax.experimental.pallas import tpu as pltpu
from jax.sharding import PartitionSpec as P

TILE = 512
MICRO = 2


def ffn_body(normed_ref, win_ref, wout_ref, out_ref, acc_ref):
    step = pl.program_id(0)

    @pl.when(step == 0)
    def _():
        acc_ref[...] = jnp.zeros_like(acc_ref)

    pre = jnp.dot(normed_ref[...], win_ref[0], preferred_element_type=jnp.float32)
    hidden = (0.5 * pre * (1.0 + lax.erf(pre * 0.7071067811865476))).astype(jnp.bfloat16)
    acc_ref[...] += lax.dot_general(
        hidden, wout_ref[0], (((1,), (1,)), ((), ())), preferred_element_type=jnp.float32
    )

    @pl.when(step == pl.num_programs(0) - 1)
    def _():
        out_ref[...] = acc_ref[...].astype(out_ref.dtype)


def ffn(normed, gathered, interpret=False):
    rows, width = normed.shape
    hidden_units = gathered.shape[2]
    return pl.pallas_call(
        ffn_body,
        grid=(hidden_units // TILE,),
        in_specs=[
            pl.BlockSpec((rows, width), lambda j: (0, 0)),
            pl.BlockSpec((1, width, TILE), lambda j: (0, 0, j)),
            pl.BlockSpec((1, width, TILE), lambda j: (1, 0, j)),
        ],
        out_specs=pl.BlockSpec((rows, width), lambda j: (0, 0)),
        out_shape=jax.ShapeDtypeStruct((rows, width), jnp.bfloat16),
        scratch_shapes=[pltpu.VMEM((rows, width), jnp.float32)],
        compiler_params=pltpu.CompilerParams(vmem_limit_bytes=48 << 20),
        cost_estimate=pl.CostEstimate(
            flops=4 * rows * width * hidden_units,
            transcendentals=rows * hidden_units,
            bytes_accessed=2 * (2 * width * hidden_units + 2 * rows * width),
        ),
        interpret=interpret,
    )(normed, gathered, gathered)


def passed_along(value, axis, steps):
    count = lax.axis_size(axis)
    first, last = (max(0, -steps), min(count, count - steps))
    return lax.ppermute(value, axis, [(source, source + steps) for source in range(first, last)])


def per_device(frames, frame_count, norm_gain, weight_in, weight_out):
    segment_count = lax.axis_size("section")
    segment_index = lax.axis_index("section")
    half_index = lax.axis_index("mp")
    both = jnp.stack([weight_in[0], weight_out[0].T])
    gathered = lax.all_gather(both, "dp", axis=1, tiled=True)
    gain_row = norm_gain[0]
    local_rows, width_local = frames.shape
    live_count = frame_count[0]
    row_ids = jnp.arange(local_rows, dtype=jnp.int32)
    first = jnp.where((row_ids < live_count)[:, None], frames, jnp.zeros_like(frames))

    def apply_layer(current):
        partner = lax.ppermute(current, "mp", [(0, 1), (1, 0)])
        whole = jnp.where(
            half_index == 0,
            jnp.concatenate([current, partner], axis=1),
            jnp.concatenate([partner, current], axis=1),
        )
        wide = whole.astype(jnp.float32)
        meansq = jnp.mean(wide * wide, axis=-1, keepdims=True)
        normed = (wide * lax.rsqrt(meansq + 1e-06) * gain_row).astype(jnp.bfloat16)
        partial_term = ffn(normed, gathered)
        keep = lax.dynamic_slice_in_dim(partial_term, half_index * width_local, width_local, axis=1)
        send = lax.dynamic_slice_in_dim(
            partial_term, (1 - half_index) * width_local, width_local, axis=1
        )
        other = lax.ppermute(send, "mp", [(0, 1), (1, 0)])
        summed = keep.astype(jnp.float32) + other.astype(jnp.float32)
        return (current.astype(jnp.float32) + summed).astype(jnp.bfloat16)

    block_rows = local_rows // MICRO
    pieces = [first[index * block_rows:(index + 1) * block_rows] for index in range(MICRO)]
    kept = [jnp.zeros_like(piece) for piece in pieces]
    for moment in range(segment_count):
        results = [apply_layer(piece) for piece in pieces]
        kept = [jnp.where(segment_index == moment, r, k) for r, k in zip(results, kept)]
        if moment + 1 < segment_count:
            pieces = [passed_along(r, "section", 1) for r in results]
    stored = jnp.concatenate(kept, axis=0)
    return stored.reshape(1, local_rows, width_local)


def solution(mesh):
    in_specs = (
        P("dp", "mp"),
        P("dp"),
        P("section", None),
        P("section", "dp", "mp"),
        P("section", "mp", "dp"),
    )
    out_specs = P("section", "dp", "mp")
    return jax.shard_map(
        per_device, mesh=mesh, in_specs=in_specs, out_specs=out_specs, check_vma=False
    )
```

```python
import jax
import jax.numpy as jnp
from jax import lax
from jax.experimental import pallas as pl
from jax.experimental.pallas import tpu as pltpu
from jax.sharding import PartitionSpec as P

TILE = 512


def ffn_body(normed_ref, win_ref, wout_ref, out_ref, acc_ref):
    step = pl.program_id(0)

    @pl.when(step == 0)
    def _():
        acc_ref[...] = jnp.zeros_like(acc_ref)

    pre = jnp.dot(normed_ref[...], win_ref[0], preferred_element_type=jnp.float32)
    hidden = (0.5 * pre * (1.0 + lax.erf(pre * 0.7071067811865476))).astype(jnp.bfloat16)
    acc_ref[...] += lax.dot_general(
        hidden, wout_ref[0], (((1,), (1,)), ((), ())), preferred_element_type=jnp.float32
    )

    @pl.when(step == pl.num_programs(0) - 1)
    def _():
        out_ref[...] = acc_ref[...].astype(out_ref.dtype)


def ffn(normed, gathered, interpret=False):
    rows, width = normed.shape
    hidden_units = gathered.shape[2]
    return pl.pallas_call(
        ffn_body,
        grid=(hidden_units // TILE,),
        in_specs=[
            pl.BlockSpec((rows, width), lambda j: (0, 0)),
            pl.BlockSpec((1, width, TILE), lambda j: (0, 0, j)),
            pl.BlockSpec((1, width, TILE), lambda j: (1, 0, j)),
        ],
        out_specs=pl.BlockSpec((rows, width), lambda j: (0, 0)),
        out_shape=jax.ShapeDtypeStruct((rows, width), jnp.bfloat16),
        scratch_shapes=[pltpu.VMEM((rows, width), jnp.float32)],
        compiler_params=pltpu.CompilerParams(vmem_limit_bytes=48 << 20),
        interpret=interpret,
    )(normed, gathered, gathered)


def passed_along(value, axis, steps):
    count = lax.axis_size(axis)
    first, last = (max(0, -steps), min(count, count - steps))
    return lax.ppermute(value, axis, [(source, source + steps) for source in range(first, last)])


def per_device(frames, frame_count, norm_gain, weight_in, weight_out):
    segment_count = lax.axis_size("section")
    segment_index = lax.axis_index("section")
    half_index = lax.axis_index("mp")
    both = jnp.stack([weight_in[0], weight_out[0].T])
    gathered = lax.all_gather(both, "dp", axis=1, tiled=True)
    gain_row = norm_gain[0]
    local_rows, width_local = frames.shape
    live_count = frame_count[0]
    row_ids = jnp.arange(local_rows, dtype=jnp.int32)
    first = jnp.where((row_ids < live_count)[:, None], frames, jnp.zeros_like(frames))

    def apply_layer(current):
        partner = lax.ppermute(current, "mp", [(0, 1), (1, 0)])
        whole = jnp.where(
            half_index == 0,
            jnp.concatenate([current, partner], axis=1),
            jnp.concatenate([partner, current], axis=1),
        )
        wide = whole.astype(jnp.float32)
        meansq = jnp.mean(wide * wide, axis=-1, keepdims=True)
        normed = (wide * lax.rsqrt(meansq + 1e-06) * gain_row).astype(jnp.bfloat16)
        partial_term = ffn(normed, gathered)
        keep = lax.dynamic_slice_in_dim(partial_term, half_index * width_local, width_local, axis=1)
        send = lax.dynamic_slice_in_dim(
            partial_term, (1 - half_index) * width_local, width_local, axis=1
        )
        other = lax.ppermute(send, "mp", [(0, 1), (1, 0)])
        summed = keep.astype(jnp.float32) + other.astype(jnp.float32)
        return (current.astype(jnp.float32) + summed).astype(jnp.bfloat16)

    result = apply_layer(first)
    stored = jnp.where(segment_index == 0, result, jnp.zeros_like(result))

    for moment in range(1, segment_count):
        result = apply_layer(passed_along(result, "section", 1))
        stored = jnp.where(segment_index == moment, result, stored)
    return stored.reshape(1, local_rows, width_local)


def solution(mesh):
    in_specs = (
        P("dp", "mp"),
        P("dp"),
        P("section", None),
        P("section", "dp", "mp"),
        P("section", "mp", "dp"),
    )
    out_specs = P("section", "dp", "mp")
    return jax.shard_map(
        per_device, mesh=mesh, in_specs=in_specs, out_specs=out_specs, check_vma=False
    )
```

```python
import jax
import jax.numpy as jnp
from jax import lax
from jax.experimental import pallas as pl
from jax.experimental.pallas import tpu as pltpu
from jax.sharding import PartitionSpec as P

TILE = 512


def ffn_body(normed_ref, win_ref, wout_ref, keep_ref, send_ref, acc_ref):
    step = pl.program_id(0)

    @pl.when(step == 0)
    def _():
        acc_ref[...] = jnp.zeros_like(acc_ref)

    pre = jnp.dot(normed_ref[...], win_ref[0], preferred_element_type=jnp.float32)
    hidden = (0.5 * pre * (1.0 + lax.erf(pre * 0.7071067811865476))).astype(jnp.bfloat16)
    acc_ref[...] += lax.dot_general(
        hidden, wout_ref[0], (((1,), (1,)), ((), ())), preferred_element_type=jnp.float32
    )

    @pl.when(step == pl.num_programs(0) - 1)
    def _():
        half = keep_ref.shape[1]
        own = lax.axis_index("mp")
        keep_ref[...] = acc_ref[:, pl.ds(pl.multiple_of(own * half, 128), half)].astype(keep_ref.dtype)
        send_ref[...] = acc_ref[:, pl.ds(pl.multiple_of((1 - own) * half, 128), half)].astype(
            send_ref.dtype
        )


def ffn(normed, gathered):
    rows, width = normed.shape
    hidden_units = gathered.shape[2]
    half = width // 2
    return pl.pallas_call(
        ffn_body,
        grid=(hidden_units // TILE,),
        in_specs=[
            pl.BlockSpec((rows, width), lambda j: (0, 0)),
            pl.BlockSpec((1, width, TILE), lambda j: (0, 0, j)),
            pl.BlockSpec((1, width, TILE), lambda j: (1, 0, j)),
        ],
        out_specs=[
            pl.BlockSpec((rows, half), lambda j: (0, 0)),
            pl.BlockSpec((rows, half), lambda j: (0, 0)),
        ],
        out_shape=[jax.ShapeDtypeStruct((rows, half), jnp.bfloat16)] * 2,
        scratch_shapes=[pltpu.VMEM((rows, width), jnp.float32)],
        compiler_params=pltpu.CompilerParams(vmem_limit_bytes=48 << 20),
    )(normed, gathered, gathered)


def passed_along(value, axis, steps):
    count = lax.axis_size(axis)
    first, last = (max(0, -steps), min(count, count - steps))
    return lax.ppermute(value, axis, [(source, source + steps) for source in range(first, last)])


def per_device(frames, frame_count, norm_gain, weight_in, weight_out):
    segment_count = lax.axis_size("section")
    segment_index = lax.axis_index("section")
    half_index = lax.axis_index("mp")
    both = jnp.stack([weight_in[0], weight_out[0].T])
    gathered = lax.all_gather(both, "dp", axis=1, tiled=True)
    gain_row = norm_gain[0]
    local_rows, width_local = frames.shape
    live_count = frame_count[0]
    row_ids = jnp.arange(local_rows, dtype=jnp.int32)
    first = jnp.where((row_ids < live_count)[:, None], frames, jnp.zeros_like(frames))

    def apply_layer(current):
        partner = lax.ppermute(current, "mp", [(0, 1), (1, 0)])
        whole = jnp.where(
            half_index == 0,
            jnp.concatenate([current, partner], axis=1),
            jnp.concatenate([partner, current], axis=1),
        )
        wide = whole.astype(jnp.float32)
        meansq = jnp.mean(wide * wide, axis=-1, keepdims=True)
        normed = (wide * lax.rsqrt(meansq + 1e-06) * gain_row).astype(jnp.bfloat16)
        keep, send = ffn(normed, gathered)
        other = lax.ppermute(send, "mp", [(0, 1), (1, 0)])
        summed = keep.astype(jnp.float32) + other.astype(jnp.float32)
        return (current.astype(jnp.float32) + summed).astype(jnp.bfloat16)

    result = apply_layer(first)
    stored = jnp.where(segment_index == 0, result, jnp.zeros_like(result))

    for moment in range(1, segment_count):
        result = apply_layer(passed_along(result, "section", 1))
        stored = lax.optimization_barrier(jnp.where(segment_index == moment, result, stored))
    return stored.reshape(1, local_rows, width_local)


def solution(mesh):
    in_specs = (
        P("dp", "mp"),
        P("dp"),
        P("section", None),
        P("section", "dp", "mp"),
        P("section", "mp", "dp"),
    )
    out_specs = P("section", "dp", "mp")
    return jax.shard_map(
        per_device, mesh=mesh, in_specs=in_specs, out_specs=out_specs, check_vma=False
    )
```

```python
import jax
import jax.numpy as jnp
from jax import lax
from jax.experimental import pallas as pl
from jax.experimental.pallas import tpu as pltpu
from jax.sharding import PartitionSpec as P

TILE = 512


def ffn_body(own_ref, partner_ref, gain_ref, win_ref, wout_ref, keep_ref, send_ref, normed_ref, acc_ref):
    step = pl.program_id(0)
    half = keep_ref.shape[1]
    own = lax.axis_index("mp")
    own_cols = pl.ds(pl.multiple_of(own * half, 128), half)
    other_cols = pl.ds(pl.multiple_of((1 - own) * half, 128), half)

    @pl.when(step == 0)
    def _():
        mine = own_ref[...].astype(jnp.float32)
        theirs = partner_ref[...].astype(jnp.float32)
        total = jnp.sum(mine * mine, axis=-1, keepdims=True) + jnp.sum(
            theirs * theirs, axis=-1, keepdims=True
        )
        scale = lax.rsqrt(total / (2 * half) + 1e-06)
        normed_ref[:, own_cols] = (mine * scale * gain_ref[:, own_cols]).astype(normed_ref.dtype)
        normed_ref[:, other_cols] = (theirs * scale * gain_ref[:, other_cols]).astype(
            normed_ref.dtype
        )
        acc_ref[...] = jnp.zeros_like(acc_ref)

    pre = jnp.dot(normed_ref[...], win_ref[0], preferred_element_type=jnp.float32)
    hidden = (0.5 * pre * (1.0 + lax.erf(pre * 0.7071067811865476))).astype(jnp.bfloat16)
    acc_ref[...] += lax.dot_general(
        hidden, wout_ref[0], (((1,), (1,)), ((), ())), preferred_element_type=jnp.float32
    )

    @pl.when(step == pl.num_programs(0) - 1)
    def _():
        keep_ref[...] = acc_ref[:, own_cols].astype(keep_ref.dtype)
        send_ref[...] = acc_ref[:, other_cols].astype(send_ref.dtype)


def ffn(current, partner, gain, gathered):
    rows, half = current.shape
    width = 2 * half
    hidden_units = gathered.shape[2]
    return pl.pallas_call(
        ffn_body,
        grid=(hidden_units // TILE,),
        in_specs=[
            pl.BlockSpec((rows, half), lambda j: (0, 0)),
            pl.BlockSpec((rows, half), lambda j: (0, 0)),
            pl.BlockSpec((1, width), lambda j: (0, 0)),
            pl.BlockSpec((1, width, TILE), lambda j: (0, 0, j)),
            pl.BlockSpec((1, width, TILE), lambda j: (1, 0, j)),
        ],
        out_specs=[
            pl.BlockSpec((rows, half), lambda j: (0, 0)),
            pl.BlockSpec((rows, half), lambda j: (0, 0)),
        ],
        out_shape=[jax.ShapeDtypeStruct((rows, half), jnp.bfloat16)] * 2,
        scratch_shapes=[
            pltpu.VMEM((rows, width), jnp.bfloat16),
            pltpu.VMEM((rows, width), jnp.float32),
        ],
        compiler_params=pltpu.CompilerParams(vmem_limit_bytes=48 << 20),
    )(current, partner, gain, gathered, gathered)


def passed_along(value, axis, steps):
    count = lax.axis_size(axis)
    first, last = (max(0, -steps), min(count, count - steps))
    return lax.ppermute(value, axis, [(source, source + steps) for source in range(first, last)])


def per_device(frames, frame_count, norm_gain, weight_in, weight_out):
    segment_count = lax.axis_size("section")
    segment_index = lax.axis_index("section")
    half_index = lax.axis_index("mp")
    both = jnp.stack([weight_in[0], weight_out[0].T])
    gathered = lax.all_gather(both, "dp", axis=1, tiled=True)
    local_rows, width_local = frames.shape
    live_count = frame_count[0]
    row_ids = jnp.arange(local_rows, dtype=jnp.int32)
    first = jnp.where((row_ids < live_count)[:, None], frames, jnp.zeros_like(frames))

    def apply_layer(current):
        partner = lax.ppermute(current, "mp", [(0, 1), (1, 0)])
        keep, send = ffn(current, partner, norm_gain, gathered)
        other = lax.ppermute(send, "mp", [(0, 1), (1, 0)])
        summed = keep.astype(jnp.float32) + other.astype(jnp.float32)
        return (current.astype(jnp.float32) + summed).astype(jnp.bfloat16)

    result = apply_layer(first)
    stored = jnp.where(segment_index == 0, result, jnp.zeros_like(result))

    for moment in range(1, segment_count):
        result = apply_layer(passed_along(result, "section", 1))
        stored = lax.optimization_barrier(jnp.where(segment_index == moment, result, stored))
    return stored.reshape(1, local_rows, width_local)


def solution(mesh):
    in_specs = (
        P("dp", "mp"),
        P("dp"),
        P("section", None),
        P("section", "dp", "mp"),
        P("section", "mp", "dp"),
    )
    out_specs = P("section", "dp", "mp")
    return jax.shard_map(
        per_device, mesh=mesh, in_specs=in_specs, out_specs=out_specs, check_vma=False
    )
```

```python
import jax
import jax.numpy as jnp
from jax import lax
from jax.experimental import pallas as pl
from jax.experimental.pallas import tpu as pltpu
from jax.sharding import PartitionSpec as P

TILE = 512


def ffn_body(own_ref, partner_ref, gain_ref, win_ref, wout_ref, keep_ref, send_ref, normed_ref, acc_ref):
    step = pl.program_id(0)
    half = keep_ref.shape[1]
    own = lax.axis_index("mp")
    own_cols = pl.ds(pl.multiple_of(own * half, 128), half)
    other_cols = pl.ds(pl.multiple_of((1 - own) * half, 128), half)

    @pl.when(step == 0)
    def _():
        mine = own_ref[...].astype(jnp.float32)
        theirs = partner_ref[...].astype(jnp.float32)
        total = jnp.sum(mine * mine, axis=-1, keepdims=True) + jnp.sum(
            theirs * theirs, axis=-1, keepdims=True
        )
        scale = lax.rsqrt(total / (2 * half) + 1e-06)
        normed_ref[:, own_cols] = (mine * scale * gain_ref[:, own_cols]).astype(normed_ref.dtype)
        normed_ref[:, other_cols] = (theirs * scale * gain_ref[:, other_cols]).astype(
            normed_ref.dtype
        )
        acc_ref[...] = jnp.zeros_like(acc_ref)

    pre = jnp.dot(normed_ref[...], win_ref[0], preferred_element_type=jnp.float32)
    hidden = (0.5 * pre * (1.0 + lax.erf(pre * 0.7071067811865476))).astype(jnp.bfloat16)
    acc_ref[...] += lax.dot_general(
        hidden, wout_ref[0], (((1,), (1,)), ((), ())), preferred_element_type=jnp.float32
    )

    @pl.when(step == pl.num_programs(0) - 1)
    def _():
        keep_ref[...] = acc_ref[:, own_cols].astype(keep_ref.dtype)
        send_ref[...] = acc_ref[:, other_cols].astype(send_ref.dtype)


def ffn(current, partner, gain, gathered):
    rows, half = current.shape
    width = 2 * half
    hidden_units = gathered.shape[2]
    return pl.pallas_call(
        ffn_body,
        grid=(hidden_units // TILE,),
        in_specs=[
            pl.BlockSpec((rows, half), lambda j: (0, 0)),
            pl.BlockSpec((rows, half), lambda j: (0, 0)),
            pl.BlockSpec((1, width), lambda j: (0, 0)),
            pl.BlockSpec((1, width, TILE), lambda j: (0, 0, j)),
            pl.BlockSpec((1, width, TILE), lambda j: (1, 0, j)),
        ],
        out_specs=[
            pl.BlockSpec((rows, half), lambda j: (0, 0)),
            pl.BlockSpec((rows, half), lambda j: (0, 0)),
        ],
        out_shape=[jax.ShapeDtypeStruct((rows, half), jnp.bfloat16)] * 2,
        scratch_shapes=[
            pltpu.VMEM((rows, width), jnp.bfloat16),
            pltpu.VMEM((rows, width), jnp.float32),
        ],
        compiler_params=pltpu.CompilerParams(vmem_limit_bytes=48 << 20),
    )(current, partner, gain, gathered, gathered)


def passed_along(value, axis, steps):
    count = lax.axis_size(axis)
    return lax.ppermute(value, axis, [(source, (source + steps) % count) for source in range(count)])


def per_device(frames, frame_count, norm_gain, weight_in, weight_out):
    segment_count = lax.axis_size("section")
    segment_index = lax.axis_index("section")
    half_index = lax.axis_index("mp")
    both = jnp.stack([weight_in[0], weight_out[0].T])
    gathered = lax.all_gather(both, "dp", axis=1, tiled=True)
    local_rows, width_local = frames.shape
    live_count = frame_count[0]
    row_ids = jnp.arange(local_rows, dtype=jnp.int32)
    first = jnp.where((row_ids < live_count)[:, None], frames, jnp.zeros_like(frames))

    def apply_layer(current):
        partner = lax.ppermute(current, "mp", [(0, 1), (1, 0)])
        keep, send = ffn(current, partner, norm_gain, gathered)
        other = lax.ppermute(send, "mp", [(0, 1), (1, 0)])
        summed = keep.astype(jnp.float32) + other.astype(jnp.float32)
        return (current.astype(jnp.float32) + summed).astype(jnp.bfloat16)

    result = apply_layer(first)
    stored = jnp.where(segment_index == 0, result, jnp.zeros_like(result))

    for moment in range(1, segment_count):
        result = apply_layer(passed_along(result, "section", 1))
        stored = lax.optimization_barrier(jnp.where(segment_index == moment, result, stored))
    return stored.reshape(1, local_rows, width_local)


def solution(mesh):
    in_specs = (
        P("dp", "mp"),
        P("dp"),
        P("section", None),
        P("section", "dp", "mp"),
        P("section", "mp", "dp"),
    )
    out_specs = P("section", "dp", "mp")
    return jax.shard_map(
        per_device, mesh=mesh, in_specs=in_specs, out_specs=out_specs, check_vma=False
    )
```

```python
import jax
import jax.numpy as jnp
from jax import lax
from jax.experimental import pallas as pl
from jax.experimental.pallas import tpu as pltpu
from jax.sharding import PartitionSpec as P

TILE = 512


def ffn_body(own_ref, partner_ref, gain_ref, win_ref, wout_ref, keep_ref, send_ref, normed_ref, acc_ref):
    step = pl.program_id(0)
    half = keep_ref.shape[1]
    own = lax.axis_index("mp")
    own_cols = pl.ds(pl.multiple_of(own * half, 128), half)
    other_cols = pl.ds(pl.multiple_of((1 - own) * half, 128), half)

    @pl.when(step == 0)
    def _():
        mine = own_ref[...].astype(jnp.float32)
        theirs = partner_ref[...].astype(jnp.float32)
        total = jnp.sum(mine * mine, axis=-1, keepdims=True) + jnp.sum(
            theirs * theirs, axis=-1, keepdims=True
        )
        scale = lax.rsqrt(total / (2 * half) + 1e-06)
        normed_ref[:, own_cols] = (mine * scale * gain_ref[:, own_cols]).astype(normed_ref.dtype)
        normed_ref[:, other_cols] = (theirs * scale * gain_ref[:, other_cols]).astype(
            normed_ref.dtype
        )
        acc_ref[...] = jnp.zeros_like(acc_ref)

    pre = jnp.dot(normed_ref[...], win_ref[0], preferred_element_type=jnp.float32)
    hidden = (0.5 * pre * (1.0 + lax.erf(pre * 0.7071067811865476))).astype(jnp.bfloat16)
    acc_ref[...] += lax.dot_general(
        hidden, wout_ref[0], (((1,), (1,)), ((), ())), preferred_element_type=jnp.float32
    )

    @pl.when(step == pl.num_programs(0) - 1)
    def _():
        keep_ref[...] = acc_ref[:, own_cols].astype(keep_ref.dtype)
        send_ref[...] = acc_ref[:, other_cols].astype(send_ref.dtype)


def ffn(current, partner, gain, gathered):
    rows, half = current.shape
    width = 2 * half
    hidden_units = gathered.shape[2]
    return pl.pallas_call(
        ffn_body,
        grid=(hidden_units // TILE,),
        in_specs=[
            pl.BlockSpec((rows, half), lambda j: (0, 0)),
            pl.BlockSpec((rows, half), lambda j: (0, 0)),
            pl.BlockSpec((1, width), lambda j: (0, 0)),
            pl.BlockSpec((1, width, TILE), lambda j: (0, 0, j)),
            pl.BlockSpec((1, width, TILE), lambda j: (1, 0, j)),
        ],
        out_specs=[
            pl.BlockSpec((rows, half), lambda j: (0, 0)),
            pl.BlockSpec((rows, half), lambda j: (0, 0)),
        ],
        out_shape=[jax.ShapeDtypeStruct((rows, half), jnp.bfloat16)] * 2,
        scratch_shapes=[
            pltpu.VMEM((rows, width), jnp.bfloat16),
            pltpu.VMEM((rows, width), jnp.float32),
        ],
        compiler_params=pltpu.CompilerParams(vmem_limit_bytes=48 << 20),
    )(current, partner, gain, gathered, gathered)


RELAYED = 32


def shifted(value, axis, steps):
    count = lax.axis_size(axis)
    return lax.ppermute(value, axis, [(source, (source + steps) % count) for source in range(count)])


def passed_along(value, axis):
    count = lax.axis_size(axis)
    direct = shifted(value[:-RELAYED], axis, 1)
    relayed = value[-RELAYED:]
    for _ in range(count - 1):
        relayed = shifted(relayed, axis, -1)
    return jnp.concatenate([direct, relayed], axis=0)


def per_device(frames, frame_count, norm_gain, weight_in, weight_out):
    segment_count = lax.axis_size("section")
    segment_index = lax.axis_index("section")
    half_index = lax.axis_index("mp")
    both = jnp.stack([weight_in[0], weight_out[0].T])
    gathered = lax.all_gather(both, "dp", axis=1, tiled=True)
    local_rows, width_local = frames.shape
    live_count = frame_count[0]
    row_ids = jnp.arange(local_rows, dtype=jnp.int32)
    first = jnp.where((row_ids < live_count)[:, None], frames, jnp.zeros_like(frames))

    def apply_layer(current):
        partner = lax.ppermute(current, "mp", [(0, 1), (1, 0)])
        keep, send = ffn(current, partner, norm_gain, gathered)
        other = lax.ppermute(send, "mp", [(0, 1), (1, 0)])
        summed = keep.astype(jnp.float32) + other.astype(jnp.float32)
        return (current.astype(jnp.float32) + summed).astype(jnp.bfloat16)

    result = apply_layer(first)
    stored = jnp.where(segment_index == 0, result, jnp.zeros_like(result))

    for moment in range(1, segment_count):
        result = apply_layer(passed_along(result, "section"))
        stored = lax.optimization_barrier(jnp.where(segment_index == moment, result, stored))
    return stored.reshape(1, local_rows, width_local)


def solution(mesh):
    in_specs = (
        P("dp", "mp"),
        P("dp"),
        P("section", None),
        P("section", "dp", "mp"),
        P("section", "mp", "dp"),
    )
    out_specs = P("section", "dp", "mp")
    return jax.shard_map(
        per_device, mesh=mesh, in_specs=in_specs, out_specs=out_specs, check_vma=False
    )
```

```python
import jax
import jax.numpy as jnp
from jax import lax
from jax.experimental import pallas as pl
from jax.experimental.pallas import tpu as pltpu
from jax.sharding import PartitionSpec as P

TILE = 512


def ffn_body(own_ref, partner_ref, gain_ref, win_ref, wout_ref, keep_ref, send_ref, normed_ref, acc_ref):
    step = pl.program_id(0)
    half = keep_ref.shape[1]
    own = lax.axis_index("mp")
    own_cols = pl.ds(pl.multiple_of(own * half, 128), half)
    other_cols = pl.ds(pl.multiple_of((1 - own) * half, 128), half)

    @pl.when(step == 0)
    def _():
        mine = own_ref[...].astype(jnp.float32)
        theirs = partner_ref[...].astype(jnp.float32)
        total = jnp.sum(mine * mine, axis=-1, keepdims=True) + jnp.sum(
            theirs * theirs, axis=-1, keepdims=True
        )
        scale = lax.rsqrt(total / (2 * half) + 1e-06)
        normed_ref[:, own_cols] = (mine * scale * gain_ref[:, own_cols]).astype(normed_ref.dtype)
        normed_ref[:, other_cols] = (theirs * scale * gain_ref[:, other_cols]).astype(
            normed_ref.dtype
        )
        acc_ref[...] = jnp.zeros_like(acc_ref)

    pre = jnp.dot(normed_ref[...], win_ref[0], preferred_element_type=jnp.float32)
    hidden = (0.5 * pre * (1.0 + lax.erf(pre * 0.7071067811865476))).astype(jnp.bfloat16)
    acc_ref[...] += lax.dot_general(
        hidden, wout_ref[0], (((1,), (1,)), ((), ())), preferred_element_type=jnp.float32
    )

    @pl.when(step == pl.num_programs(0) - 1)
    def _():
        keep_ref[...] = acc_ref[:, own_cols].astype(keep_ref.dtype)
        send_ref[...] = acc_ref[:, other_cols].astype(send_ref.dtype)


def ffn(current, partner, gain, gathered):
    rows, half = current.shape
    width = 2 * half
    hidden_units = gathered.shape[2]
    return pl.pallas_call(
        ffn_body,
        grid=(hidden_units // TILE,),
        in_specs=[
            pl.BlockSpec((rows, half), lambda j: (0, 0)),
            pl.BlockSpec((rows, half), lambda j: (0, 0)),
            pl.BlockSpec((1, width), lambda j: (0, 0)),
            pl.BlockSpec((1, width, TILE), lambda j: (0, 0, j)),
            pl.BlockSpec((1, width, TILE), lambda j: (1, 0, j)),
        ],
        out_specs=[
            pl.BlockSpec((rows, half), lambda j: (0, 0)),
            pl.BlockSpec((rows, half), lambda j: (0, 0)),
        ],
        out_shape=[jax.ShapeDtypeStruct((rows, half), jnp.bfloat16)] * 2,
        scratch_shapes=[
            pltpu.VMEM((rows, width), jnp.bfloat16),
            pltpu.VMEM((rows, width), jnp.float32),
        ],
        compiler_params=pltpu.CompilerParams(vmem_limit_bytes=48 << 20),
    )(current, partner, gain, gathered, gathered)


RELAYED = 32


def shifted(value, axis, steps):
    count = lax.axis_size(axis)
    return lax.ppermute(value, axis, [(source, (source + steps) % count) for source in range(count)])


def passed_along(value, axis):
    count = lax.axis_size(axis)
    direct = shifted(value[:-RELAYED], axis, 1)
    relayed = value[-RELAYED:]
    for _ in range(count - 1):
        relayed = shifted(relayed, axis, -1)
    return jnp.concatenate([direct, relayed], axis=0)


def per_device(frames, frame_count, norm_gain, weight_in, weight_out):
    segment_count = lax.axis_size("section")
    segment_index = lax.axis_index("section")
    half_index = lax.axis_index("mp")
    eye = jnp.eye(weight_out.shape[2], dtype=weight_out.dtype)
    out_t = lax.dot_general(
        eye, weight_out[0], (((1,), (1,)), ((), ())), preferred_element_type=jnp.float32
    ).astype(weight_out.dtype)
    both = jnp.stack([weight_in[0], out_t])
    gathered = lax.all_gather(both, "dp", axis=1, tiled=True)
    local_rows, width_local = frames.shape
    live_count = frame_count[0]
    row_ids = jnp.arange(local_rows, dtype=jnp.int32)
    first = jnp.where((row_ids < live_count)[:, None], frames, jnp.zeros_like(frames))

    def apply_layer(current):
        partner = lax.ppermute(current, "mp", [(0, 1), (1, 0)])
        keep, send = ffn(current, partner, norm_gain, gathered)
        other = lax.ppermute(send, "mp", [(0, 1), (1, 0)])
        summed = keep.astype(jnp.float32) + other.astype(jnp.float32)
        return (current.astype(jnp.float32) + summed).astype(jnp.bfloat16)

    result = apply_layer(first)
    stored = jnp.where(segment_index == 0, result, jnp.zeros_like(result))

    for moment in range(1, segment_count):
        result = apply_layer(passed_along(result, "section"))
        stored = lax.optimization_barrier(jnp.where(segment_index == moment, result, stored))
    return stored.reshape(1, local_rows, width_local)


def solution(mesh):
    in_specs = (
        P("dp", "mp"),
        P("dp"),
        P("section", None),
        P("section", "dp", "mp"),
        P("section", "mp", "dp"),
    )
    out_specs = P("section", "dp", "mp")
    return jax.shard_map(
        per_device, mesh=mesh, in_specs=in_specs, out_specs=out_specs, check_vma=False
    )
```

```python
import jax
import jax.numpy as jnp
from jax import lax
from jax.experimental import pallas as pl
from jax.experimental.pallas import tpu as pltpu
from jax.sharding import PartitionSpec as P

TILE = 512


def ffn_body(own_ref, partner_ref, gain_ref, win_ref, wout_ref, keep_ref, send_ref, normed_ref, acc_ref):
    step = pl.program_id(0)
    half = keep_ref.shape[1]
    own = lax.axis_index("mp")
    own_cols = pl.ds(pl.multiple_of(own * half, 128), half)
    other_cols = pl.ds(pl.multiple_of((1 - own) * half, 128), half)

    @pl.when(step == 0)
    def _():
        mine = own_ref[...].astype(jnp.float32)
        theirs = partner_ref[...].astype(jnp.float32)
        total = jnp.sum(mine * mine, axis=-1, keepdims=True) + jnp.sum(
            theirs * theirs, axis=-1, keepdims=True
        )
        scale = lax.rsqrt(total / (2 * half) + 1e-06)
        normed_ref[:, own_cols] = (mine * scale * gain_ref[:, own_cols]).astype(normed_ref.dtype)
        normed_ref[:, other_cols] = (theirs * scale * gain_ref[:, other_cols]).astype(
            normed_ref.dtype
        )
        acc_ref[...] = jnp.zeros_like(acc_ref)

    blocks, _, piece, tile = win_ref.shape
    w_in = win_ref[:, 0].reshape(blocks * piece, tile)
    w_out = wout_ref[:, 0].reshape(blocks * piece, tile)
    pre = jnp.dot(normed_ref[...], w_in, preferred_element_type=jnp.float32)
    hidden = (0.5 * pre * (1.0 + lax.erf(pre * 0.7071067811865476))).astype(jnp.bfloat16)
    acc_ref[...] += lax.dot_general(
        hidden, w_out, (((1,), (1,)), ((), ())), preferred_element_type=jnp.float32
    )

    @pl.when(step == pl.num_programs(0) - 1)
    def _():
        keep_ref[...] = acc_ref[:, own_cols].astype(keep_ref.dtype)
        send_ref[...] = acc_ref[:, other_cols].astype(send_ref.dtype)


def ffn(current, partner, gain, gathered):
    rows, half = current.shape
    width = 2 * half
    blocks, _, piece, hidden_units = gathered.shape
    return pl.pallas_call(
        ffn_body,
        grid=(hidden_units // TILE,),
        in_specs=[
            pl.BlockSpec((rows, half), lambda j: (0, 0)),
            pl.BlockSpec((rows, half), lambda j: (0, 0)),
            pl.BlockSpec((1, width), lambda j: (0, 0)),
            pl.BlockSpec((blocks, 1, piece, TILE), lambda j: (0, 0, 0, j)),
            pl.BlockSpec((blocks, 1, piece, TILE), lambda j: (0, 1, 0, j)),
        ],
        out_specs=[
            pl.BlockSpec((rows, half), lambda j: (0, 0)),
            pl.BlockSpec((rows, half), lambda j: (0, 0)),
        ],
        out_shape=[jax.ShapeDtypeStruct((rows, half), jnp.bfloat16)] * 2,
        scratch_shapes=[
            pltpu.VMEM((rows, width), jnp.bfloat16),
            pltpu.VMEM((rows, width), jnp.float32),
        ],
        compiler_params=pltpu.CompilerParams(vmem_limit_bytes=48 << 20),
    )(current, partner, gain, gathered, gathered)


RELAYED = 32


def shifted(value, axis, steps):
    count = lax.axis_size(axis)
    return lax.ppermute(value, axis, [(source, (source + steps) % count) for source in range(count)])


def passed_along(value, axis):
    count = lax.axis_size(axis)
    direct = shifted(value[:-RELAYED], axis, 1)
    relayed = value[-RELAYED:]
    for _ in range(count - 1):
        relayed = shifted(relayed, axis, -1)
    return jnp.concatenate([direct, relayed], axis=0)


def per_device(frames, frame_count, norm_gain, weight_in, weight_out):
    segment_count = lax.axis_size("section")
    segment_index = lax.axis_index("section")
    half_index = lax.axis_index("mp")
    piece = weight_in.shape[1]
    both = jnp.concatenate([weight_in[0], weight_out[0].T], axis=0)
    gathered = lax.all_gather(both, "dp", axis=0, tiled=True)
    gathered = gathered.reshape(-1, 2, piece, gathered.shape[1])
    local_rows, width_local = frames.shape
    live_count = frame_count[0]
    row_ids = jnp.arange(local_rows, dtype=jnp.int32)
    first = jnp.where((row_ids < live_count)[:, None], frames, jnp.zeros_like(frames))

    def apply_layer(current):
        partner = lax.ppermute(current, "mp", [(0, 1), (1, 0)])
        keep, send = ffn(current, partner, norm_gain, gathered)
        other = lax.ppermute(send, "mp", [(0, 1), (1, 0)])
        summed = keep.astype(jnp.float32) + other.astype(jnp.float32)
        return (current.astype(jnp.float32) + summed).astype(jnp.bfloat16)

    result = apply_layer(first)
    stored = jnp.where(segment_index == 0, result, jnp.zeros_like(result))

    for moment in range(1, segment_count):
        result = apply_layer(passed_along(result, "section"))
        stored = lax.optimization_barrier(jnp.where(segment_index == moment, result, stored))
    return stored.reshape(1, local_rows, width_local)


def solution(mesh):
    in_specs = (
        P("dp", "mp"),
        P("dp"),
        P("section", None),
        P("section", "dp", "mp"),
        P("section", "mp", "dp"),
    )
    out_specs = P("section", "dp", "mp")
    return jax.shard_map(
        per_device, mesh=mesh, in_specs=in_specs, out_specs=out_specs, check_vma=False
    )
```

```python
import jax
import jax.numpy as jnp
from jax import lax
from jax.experimental import pallas as pl
from jax.experimental.pallas import tpu as pltpu
from jax.sharding import PartitionSpec as P

TILE = 512
MICRO = 2


def ffn_body(own_ref, partner_ref, gain_ref, win_ref, wout_ref, keep_ref, send_ref, normed_ref, acc_ref):
    step = pl.program_id(0)
    half = keep_ref.shape[1]
    own = lax.axis_index("mp")
    own_cols = pl.ds(pl.multiple_of(own * half, 128), half)
    other_cols = pl.ds(pl.multiple_of((1 - own) * half, 128), half)

    @pl.when(step == 0)
    def _():
        mine = own_ref[...].astype(jnp.float32)
        theirs = partner_ref[...].astype(jnp.float32)
        total = jnp.sum(mine * mine, axis=-1, keepdims=True) + jnp.sum(
            theirs * theirs, axis=-1, keepdims=True
        )
        scale = lax.rsqrt(total / (2 * half) + 1e-06)
        normed_ref[:, own_cols] = (mine * scale * gain_ref[:, own_cols]).astype(normed_ref.dtype)
        normed_ref[:, other_cols] = (theirs * scale * gain_ref[:, other_cols]).astype(
            normed_ref.dtype
        )
        acc_ref[...] = jnp.zeros_like(acc_ref)

    pre = jnp.dot(normed_ref[...], win_ref[0], preferred_element_type=jnp.float32)
    hidden = (0.5 * pre * (1.0 + lax.erf(pre * 0.7071067811865476))).astype(jnp.bfloat16)
    acc_ref[...] += lax.dot_general(
        hidden, wout_ref[0], (((1,), (1,)), ((), ())), preferred_element_type=jnp.float32
    )

    @pl.when(step == pl.num_programs(0) - 1)
    def _():
        keep_ref[...] = acc_ref[:, own_cols].astype(keep_ref.dtype)
        send_ref[...] = acc_ref[:, other_cols].astype(send_ref.dtype)


def ffn(current, partner, gain, gathered):
    rows, half = current.shape
    width = 2 * half
    hidden_units = gathered.shape[2]
    return pl.pallas_call(
        ffn_body,
        grid=(hidden_units // TILE,),
        in_specs=[
            pl.BlockSpec((rows, half), lambda j: (0, 0)),
            pl.BlockSpec((rows, half), lambda j: (0, 0)),
            pl.BlockSpec((1, width), lambda j: (0, 0)),
            pl.BlockSpec((1, width, TILE), lambda j: (0, 0, j)),
            pl.BlockSpec((1, width, TILE), lambda j: (1, 0, j)),
        ],
        out_specs=[
            pl.BlockSpec((rows, half), lambda j: (0, 0)),
            pl.BlockSpec((rows, half), lambda j: (0, 0)),
        ],
        out_shape=[jax.ShapeDtypeStruct((rows, half), jnp.bfloat16)] * 2,
        scratch_shapes=[
            pltpu.VMEM((rows, width), jnp.bfloat16),
            pltpu.VMEM((rows, width), jnp.float32),
        ],
        compiler_params=pltpu.CompilerParams(vmem_limit_bytes=48 << 20),
    )(current, partner, gain, gathered, gathered)


RELAYED = 16


def shifted(value, axis, steps):
    count = lax.axis_size(axis)
    return lax.ppermute(value, axis, [(source, (source + steps) % count) for source in range(count)])


def passed_along(value, axis):
    count = lax.axis_size(axis)
    direct = shifted(value[:-RELAYED], axis, 1)
    relayed = value[-RELAYED:]
    for _ in range(count - 1):
        relayed = shifted(relayed, axis, -1)
    return jnp.concatenate([direct, relayed], axis=0)


def per_device(frames, frame_count, norm_gain, weight_in, weight_out):
    segment_count = lax.axis_size("section")
    segment_index = lax.axis_index("section")
    half_index = lax.axis_index("mp")
    both = jnp.stack([weight_in[0], weight_out[0].T])
    gathered = lax.all_gather(both, "dp", axis=1, tiled=True)
    local_rows, width_local = frames.shape
    live_count = frame_count[0]
    row_ids = jnp.arange(local_rows, dtype=jnp.int32)
    first = jnp.where((row_ids < live_count)[:, None], frames, jnp.zeros_like(frames))

    def apply_layer(current):
        partner = lax.ppermute(current, "mp", [(0, 1), (1, 0)])
        keep, send = ffn(current, partner, norm_gain, gathered)
        other = lax.ppermute(send, "mp", [(0, 1), (1, 0)])
        summed = keep.astype(jnp.float32) + other.astype(jnp.float32)
        return (current.astype(jnp.float32) + summed).astype(jnp.bfloat16)

    block_rows = local_rows // MICRO
    pieces = [first[index * block_rows:(index + 1) * block_rows] for index in range(MICRO)]
    stored = jnp.zeros((MICRO, block_rows, width_local), jnp.bfloat16)
    result = None
    for moment in range(MICRO + segment_count - 1):
        own_piece = pieces[min(moment, MICRO - 1)]
        if result is None:
            current = own_piece
        else:
            current = jnp.where(segment_index == 0, own_piece, passed_along(result, "section"))
        result = apply_layer(current)
        position = moment - segment_index
        active = jnp.logical_and(position >= 0, position < MICRO)
        target = jnp.clip(position, 0, MICRO - 1)
        updated = lax.dynamic_update_index_in_dim(stored, result, target, 0)
        stored = lax.optimization_barrier(jnp.where(active, updated, stored))
    return stored.reshape(1, local_rows, width_local)


def solution(mesh):
    in_specs = (
        P("dp", "mp"),
        P("dp"),
        P("section", None),
        P("section", "dp", "mp"),
        P("section", "mp", "dp"),
    )
    out_specs = P("section", "dp", "mp")
    return jax.shard_map(
        per_device, mesh=mesh, in_specs=in_specs, out_specs=out_specs, check_vma=False
    )
```

```python
import jax
import jax.numpy as jnp
from jax import lax
from jax.experimental import pallas as pl
from jax.experimental.pallas import tpu as pltpu
from jax.sharding import PartitionSpec as P

TILE = 512
MICRO = 2


def ffn_body(own_ref, partner_ref, gain_ref, win_ref, wout_ref, keep_ref, send_ref, normed_ref, acc_ref):
    step = pl.program_id(0)
    half = keep_ref.shape[1]
    own = lax.axis_index("mp")
    own_cols = pl.ds(pl.multiple_of(own * half, 128), half)
    other_cols = pl.ds(pl.multiple_of((1 - own) * half, 128), half)

    @pl.when(step == 0)
    def _():
        mine = own_ref[...].astype(jnp.float32)
        theirs = partner_ref[...].astype(jnp.float32)
        total = jnp.sum(mine * mine, axis=-1, keepdims=True) + jnp.sum(
            theirs * theirs, axis=-1, keepdims=True
        )
        scale = lax.rsqrt(total / (2 * half) + 1e-06)
        normed_ref[:, own_cols] = (mine * scale * gain_ref[:, own_cols]).astype(normed_ref.dtype)
        normed_ref[:, other_cols] = (theirs * scale * gain_ref[:, other_cols]).astype(
            normed_ref.dtype
        )
        acc_ref[...] = jnp.zeros_like(acc_ref)

    pre = jnp.dot(normed_ref[...], win_ref[0], preferred_element_type=jnp.float32)
    hidden = (0.5 * pre * (1.0 + lax.erf(pre * 0.7071067811865476))).astype(jnp.bfloat16)
    acc_ref[...] += lax.dot_general(
        hidden, wout_ref[0], (((1,), (1,)), ((), ())), preferred_element_type=jnp.float32
    )

    @pl.when(step == pl.num_programs(0) - 1)
    def _():
        keep_ref[...] = acc_ref[:, own_cols].astype(keep_ref.dtype)
        send_ref[...] = acc_ref[:, other_cols].astype(send_ref.dtype)


def ffn(current, partner, gain, gathered):
    rows, half = current.shape
    width = 2 * half
    hidden_units = gathered.shape[2]
    return pl.pallas_call(
        ffn_body,
        grid=(hidden_units // TILE,),
        in_specs=[
            pl.BlockSpec((rows, half), lambda j: (0, 0)),
            pl.BlockSpec((rows, half), lambda j: (0, 0)),
            pl.BlockSpec((1, width), lambda j: (0, 0)),
            pl.BlockSpec((1, width, TILE), lambda j: (0, 0, j)),
            pl.BlockSpec((1, width, TILE), lambda j: (1, 0, j)),
        ],
        out_specs=[
            pl.BlockSpec((rows, half), lambda j: (0, 0)),
            pl.BlockSpec((rows, half), lambda j: (0, 0)),
        ],
        out_shape=[jax.ShapeDtypeStruct((rows, half), jnp.bfloat16)] * 2,
        scratch_shapes=[
            pltpu.VMEM((rows, width), jnp.bfloat16),
            pltpu.VMEM((rows, width), jnp.float32),
        ],
        compiler_params=pltpu.CompilerParams(vmem_limit_bytes=48 << 20),
    )(current, partner, gain, gathered, gathered)


def shifted(value, axis, steps):
    count = lax.axis_size(axis)
    return lax.ppermute(value, axis, [(source, (source + steps) % count) for source in range(count)])


def per_device(frames, frame_count, norm_gain, weight_in, weight_out):
    segment_count = lax.axis_size("section")
    segment_index = lax.axis_index("section")
    half_index = lax.axis_index("mp")
    both = jnp.stack([weight_in[0], weight_out[0].T])
    gathered = lax.all_gather(both, "dp", axis=1, tiled=True)
    local_rows, width_local = frames.shape
    live_count = frame_count[0]
    row_ids = jnp.arange(local_rows, dtype=jnp.int32)
    first = jnp.where((row_ids < live_count)[:, None], frames, jnp.zeros_like(frames))

    def apply_layer(current):
        partner = lax.ppermute(current, "mp", [(0, 1), (1, 0)])
        keep, send = ffn(current, partner, norm_gain, gathered)
        other = lax.ppermute(send, "mp", [(0, 1), (1, 0)])
        summed = keep.astype(jnp.float32) + other.astype(jnp.float32)
        return (current.astype(jnp.float32) + summed).astype(jnp.bfloat16)

    block_rows = local_rows // MICRO
    pieces = [first[index * block_rows:(index + 1) * block_rows] for index in range(MICRO)]
    stored = jnp.zeros((MICRO, block_rows, width_local), jnp.bfloat16)
    result = None
    for moment in range(MICRO + segment_count - 1):
        own_piece = pieces[min(moment, MICRO - 1)]
        if result is None:
            current = own_piece
        else:
            current = jnp.where(segment_index == 0, own_piece, shifted(result, "section", 1))
        result = apply_layer(current)
        position = moment - segment_index
        active = jnp.logical_and(position >= 0, position < MICRO)
        target = jnp.clip(position, 0, MICRO - 1)
        updated = lax.dynamic_update_index_in_dim(stored, result, target, 0)
        stored = lax.optimization_barrier(jnp.where(active, updated, stored))
    return stored.reshape(1, local_rows, width_local)


def solution(mesh):
    in_specs = (
        P("dp", "mp"),
        P("dp"),
        P("section", None),
        P("section", "dp", "mp"),
        P("section", "mp", "dp"),
    )
    out_specs = P("section", "dp", "mp")
    return jax.shard_map(
        per_device, mesh=mesh, in_specs=in_specs, out_specs=out_specs, check_vma=False
    )
```

```python
import jax
import jax.numpy as jnp
from jax import lax
from jax.experimental import pallas as pl
from jax.experimental.pallas import tpu as pltpu
from jax.sharding import PartitionSpec as P

TILE = 512


def ffn_body(own_ref, partner_ref, gain_ref, win_ref, wout_ref, keep_ref, send_ref, normed_ref, acc_ref):
    step = pl.program_id(0)
    half = keep_ref.shape[1]
    own = lax.axis_index("mp")
    own_cols = pl.ds(pl.multiple_of(own * half, 128), half)
    other_cols = pl.ds(pl.multiple_of((1 - own) * half, 128), half)

    @pl.when(step == 0)
    def _():
        mine = own_ref[...].astype(jnp.float32)
        theirs = partner_ref[...].astype(jnp.float32)
        total = jnp.sum(mine * mine, axis=-1, keepdims=True) + jnp.sum(
            theirs * theirs, axis=-1, keepdims=True
        )
        scale = lax.rsqrt(total / (2 * half) + 1e-06)
        normed_ref[:, own_cols] = (mine * scale * gain_ref[:, own_cols]).astype(normed_ref.dtype)
        normed_ref[:, other_cols] = (theirs * scale * gain_ref[:, other_cols]).astype(
            normed_ref.dtype
        )
        acc_ref[...] = jnp.zeros_like(acc_ref)

    pre = jnp.dot(normed_ref[...], win_ref[0], preferred_element_type=jnp.float32)
    hidden = (0.5 * pre * (1.0 + lax.erf(pre * 0.7071067811865476))).astype(jnp.bfloat16)
    acc_ref[...] += lax.dot_general(
        hidden, wout_ref[0], (((1,), (1,)), ((), ())), preferred_element_type=jnp.float32
    )

    @pl.when(step == pl.num_programs(0) - 1)
    def _():
        keep_ref[...] = acc_ref[:, own_cols].astype(keep_ref.dtype)
        send_ref[...] = acc_ref[:, other_cols].astype(send_ref.dtype)


def ffn(current, partner, gain, gathered):
    rows, half = current.shape
    width = 2 * half
    hidden_units = gathered.shape[2]
    return pl.pallas_call(
        ffn_body,
        grid=(hidden_units // TILE,),
        in_specs=[
            pl.BlockSpec((rows, half), lambda j: (0, 0)),
            pl.BlockSpec((rows, half), lambda j: (0, 0)),
            pl.BlockSpec((1, width), lambda j: (0, 0)),
            pl.BlockSpec((1, width, TILE), lambda j: (0, 0, j)),
            pl.BlockSpec((1, width, TILE), lambda j: (1, 0, j)),
        ],
        out_specs=[
            pl.BlockSpec((rows, half), lambda j: (0, 0)),
            pl.BlockSpec((rows, half), lambda j: (0, 0)),
        ],
        out_shape=[jax.ShapeDtypeStruct((rows, half), jnp.bfloat16)] * 2,
        scratch_shapes=[
            pltpu.VMEM((rows, width), jnp.bfloat16),
            pltpu.VMEM((rows, width), jnp.float32),
        ],
        compiler_params=pltpu.CompilerParams(vmem_limit_bytes=48 << 20),
    )(current, partner, gain, gathered, gathered)


RELAYED = 40


def shifted(value, axis, steps):
    count = lax.axis_size(axis)
    return lax.ppermute(value, axis, [(source, (source + steps) % count) for source in range(count)])


def passed_along(value, axis):
    direct = shifted(value[:-RELAYED], axis, 1)
    relayed = value[-RELAYED:]
    relayed = shifted(shifted(relayed, axis, -1), axis, 2)
    return jnp.concatenate([direct, relayed], axis=0)


def per_device(frames, frame_count, norm_gain, weight_in, weight_out):
    segment_count = lax.axis_size("section")
    segment_index = lax.axis_index("section")
    half_index = lax.axis_index("mp")
    both = jnp.stack([weight_in[0], weight_out[0].T])
    gathered = lax.all_gather(both, "dp", axis=1, tiled=True)
    local_rows, width_local = frames.shape
    live_count = frame_count[0]
    row_ids = jnp.arange(local_rows, dtype=jnp.int32)
    first = jnp.where((row_ids < live_count)[:, None], frames, jnp.zeros_like(frames))

    def apply_layer(current):
        partner = lax.ppermute(current, "mp", [(0, 1), (1, 0)])
        keep, send = ffn(current, partner, norm_gain, gathered)
        other = lax.ppermute(send, "mp", [(0, 1), (1, 0)])
        summed = keep.astype(jnp.float32) + other.astype(jnp.float32)
        return (current.astype(jnp.float32) + summed).astype(jnp.bfloat16)

    result = apply_layer(first)
    stored = jnp.where(segment_index == 0, result, jnp.zeros_like(result))

    for moment in range(1, segment_count):
        result = apply_layer(passed_along(result, "section"))
        stored = lax.optimization_barrier(jnp.where(segment_index == moment, result, stored))
    return stored.reshape(1, local_rows, width_local)


def solution(mesh):
    in_specs = (
        P("dp", "mp"),
        P("dp"),
        P("section", None),
        P("section", "dp", "mp"),
        P("section", "mp", "dp"),
    )
    out_specs = P("section", "dp", "mp")
    return jax.shard_map(
        per_device, mesh=mesh, in_specs=in_specs, out_specs=out_specs, check_vma=False
    )
```

```python
import jax
import jax.numpy as jnp
from jax import lax
from jax.experimental import pallas as pl
from jax.experimental.pallas import tpu as pltpu
from jax.sharding import PartitionSpec as P

TILE = 512


def ffn_body(own_ref, partner_ref, gain_ref, win_ref, wout_ref, keep_ref, send_ref, normed_ref, acc_ref):
    step = pl.program_id(0)
    half = keep_ref.shape[1]
    own = lax.axis_index("mp")
    own_cols = pl.ds(pl.multiple_of(own * half, 128), half)
    other_cols = pl.ds(pl.multiple_of((1 - own) * half, 128), half)

    @pl.when(step == 0)
    def _():
        mine = own_ref[...].astype(jnp.float32)
        theirs = partner_ref[...].astype(jnp.float32)
        total = jnp.sum(mine * mine, axis=-1, keepdims=True) + jnp.sum(
            theirs * theirs, axis=-1, keepdims=True
        )
        scale = lax.rsqrt(total / (2 * half) + 1e-06)
        normed_ref[:, own_cols] = (mine * scale * gain_ref[:, own_cols]).astype(normed_ref.dtype)
        normed_ref[:, other_cols] = (theirs * scale * gain_ref[:, other_cols]).astype(
            normed_ref.dtype
        )
        acc_ref[...] = jnp.zeros_like(acc_ref)

    pre = jnp.dot(normed_ref[...], win_ref[0], preferred_element_type=jnp.float32)
    hidden = (0.5 * pre * (1.0 + lax.erf(pre * 0.7071067811865476))).astype(jnp.bfloat16)
    acc_ref[...] += lax.dot_general(
        hidden, wout_ref[0], (((1,), (1,)), ((), ())), preferred_element_type=jnp.float32
    )

    @pl.when(step == pl.num_programs(0) - 1)
    def _():
        keep_ref[...] = acc_ref[:, own_cols].astype(keep_ref.dtype)
        send_ref[...] = acc_ref[:, other_cols].astype(send_ref.dtype)


def ffn(current, partner, gain, gathered):
    rows, half = current.shape
    width = 2 * half
    hidden_units = gathered.shape[2]
    return pl.pallas_call(
        ffn_body,
        grid=(hidden_units // TILE,),
        in_specs=[
            pl.BlockSpec((rows, half), lambda j: (0, 0)),
            pl.BlockSpec((rows, half), lambda j: (0, 0)),
            pl.BlockSpec((1, width), lambda j: (0, 0)),
            pl.BlockSpec((1, width, TILE), lambda j: (0, 0, j)),
            pl.BlockSpec((1, width, TILE), lambda j: (1, 0, j)),
        ],
        out_specs=[
            pl.BlockSpec((rows, half), lambda j: (0, 0)),
            pl.BlockSpec((rows, half), lambda j: (0, 0)),
        ],
        out_shape=[jax.ShapeDtypeStruct((rows, half), jnp.bfloat16)] * 2,
        scratch_shapes=[
            pltpu.VMEM((rows, width), jnp.bfloat16),
            pltpu.VMEM((rows, width), jnp.float32),
        ],
        compiler_params=pltpu.CompilerParams(vmem_limit_bytes=48 << 20),
    )(current, partner, gain, gathered, gathered)


RELAYED = 40


def shifted(value, axis, steps):
    count = lax.axis_size(axis)
    return lax.ppermute(value, axis, [(source, (source + steps) % count) for source in range(count)])


def passed_along(value, axis):
    count = lax.axis_size(axis)
    direct = shifted(value[:-RELAYED], axis, 1)
    relayed = value[-RELAYED:]
    for _ in range(count - 1):
        relayed = shifted(relayed, axis, -1)
    return jnp.concatenate([direct, relayed], axis=0)


def per_device(frames, frame_count, norm_gain, weight_in, weight_out):
    segment_count = lax.axis_size("section")
    segment_index = lax.axis_index("section")
    half_index = lax.axis_index("mp")
    both = jnp.stack([weight_in[0], weight_out[0].T])
    gathered = lax.all_gather(both, "dp", axis=1, tiled=True)
    local_rows, width_local = frames.shape
    live_count = frame_count[0]
    row_ids = jnp.arange(local_rows, dtype=jnp.int32)
    first = jnp.where((row_ids < live_count)[:, None], frames, jnp.zeros_like(frames))

    def apply_layer(current):
        partner = lax.ppermute(current, "mp", [(0, 1), (1, 0)])
        keep, send = ffn(current, partner, norm_gain, gathered)
        other = lax.ppermute(send, "mp", [(0, 1), (1, 0)])
        summed = keep.astype(jnp.float32) + other.astype(jnp.float32)
        return (current.astype(jnp.float32) + summed).astype(jnp.bfloat16)

    result = apply_layer(first)
    stored = jnp.where(segment_index == 0, result, jnp.zeros_like(result))

    for moment in range(1, segment_count):
        result = apply_layer(passed_along(result, "section"))
        stored = lax.optimization_barrier(jnp.where(segment_index == moment, result, stored))
    return stored.reshape(1, local_rows, width_local)


def solution(mesh):
    in_specs = (
        P("dp", "mp"),
        P("dp"),
        P("section", None),
        P("section", "dp", "mp"),
        P("section", "mp", "dp"),
    )
    out_specs = P("section", "dp", "mp")
    return jax.shard_map(
        per_device, mesh=mesh, in_specs=in_specs, out_specs=out_specs, check_vma=False
    )
```

```python
import jax
import jax.numpy as jnp
from jax import lax
from jax.experimental import pallas as pl
from jax.experimental.pallas import tpu as pltpu
from jax.sharding import PartitionSpec as P

TILE = 512


def ffn_body(own_ref, partner_ref, gain_ref, win_ref, wout_ref, keep_ref, send_ref, normed_ref, acc_ref):
    step = pl.program_id(0)
    half = keep_ref.shape[1]
    own = lax.axis_index("mp")
    own_cols = pl.ds(pl.multiple_of(own * half, 128), half)
    other_cols = pl.ds(pl.multiple_of((1 - own) * half, 128), half)

    @pl.when(step == 0)
    def _():
        mine = own_ref[...].astype(jnp.float32)
        theirs = partner_ref[...].astype(jnp.float32)
        total = jnp.sum(mine * mine, axis=-1, keepdims=True) + jnp.sum(
            theirs * theirs, axis=-1, keepdims=True
        )
        scale = lax.rsqrt(total / (2 * half) + 1e-06)
        normed_ref[:, own_cols] = (mine * scale * gain_ref[:, own_cols]).astype(normed_ref.dtype)
        normed_ref[:, other_cols] = (theirs * scale * gain_ref[:, other_cols]).astype(
            normed_ref.dtype
        )
        acc_ref[...] = jnp.zeros_like(acc_ref)

    pre = jnp.dot(normed_ref[...], win_ref[0], preferred_element_type=jnp.float32)
    hidden = (0.5 * pre * (1.0 + lax.erf(pre * 0.7071067811865476))).astype(jnp.bfloat16)
    acc_ref[...] += lax.dot_general(
        hidden, wout_ref[0], (((1,), (1,)), ((), ())), preferred_element_type=jnp.float32
    )

    @pl.when(step == pl.num_programs(0) - 1)
    def _():
        keep_ref[...] = acc_ref[:, own_cols].astype(keep_ref.dtype)
        send_ref[...] = acc_ref[:, other_cols].astype(send_ref.dtype)


def ffn(current, partner, gain, gathered):
    rows, half = current.shape
    width = 2 * half
    hidden_units = gathered.shape[2]
    return pl.pallas_call(
        ffn_body,
        grid=(hidden_units // TILE,),
        in_specs=[
            pl.BlockSpec((rows, half), lambda j: (0, 0)),
            pl.BlockSpec((rows, half), lambda j: (0, 0)),
            pl.BlockSpec((1, width), lambda j: (0, 0)),
            pl.BlockSpec((1, width, TILE), lambda j: (0, 0, j)),
            pl.BlockSpec((1, width, TILE), lambda j: (1, 0, j)),
        ],
        out_specs=[
            pl.BlockSpec((rows, half), lambda j: (0, 0)),
            pl.BlockSpec((rows, half), lambda j: (0, 0)),
        ],
        out_shape=[jax.ShapeDtypeStruct((rows, half), jnp.bfloat16)] * 2,
        scratch_shapes=[
            pltpu.VMEM((rows, width), jnp.bfloat16),
            pltpu.VMEM((rows, width), jnp.float32),
        ],
        compiler_params=pltpu.CompilerParams(vmem_limit_bytes=48 << 20),
    )(current, partner, gain, gathered, gathered)


RELAYED = 24


def shifted(value, axis, steps):
    count = lax.axis_size(axis)
    return lax.ppermute(value, axis, [(source, (source + steps) % count) for source in range(count)])


def passed_along(value, axis):
    count = lax.axis_size(axis)
    direct = shifted(value[:-RELAYED], axis, 1)
    relayed = value[-RELAYED:]
    for _ in range(count - 1):
        relayed = shifted(relayed, axis, -1)
    return jnp.concatenate([direct, relayed], axis=0)


def per_device(frames, frame_count, norm_gain, weight_in, weight_out):
    segment_count = lax.axis_size("section")
    segment_index = lax.axis_index("section")
    half_index = lax.axis_index("mp")
    both = jnp.stack([weight_in[0], weight_out[0].T])
    gathered = lax.all_gather(both, "dp", axis=1, tiled=True)
    local_rows, width_local = frames.shape
    live_count = frame_count[0]
    row_ids = jnp.arange(local_rows, dtype=jnp.int32)
    first = jnp.where((row_ids < live_count)[:, None], frames, jnp.zeros_like(frames))

    def apply_layer(current):
        partner = lax.ppermute(current, "mp", [(0, 1), (1, 0)])
        keep, send = ffn(current, partner, norm_gain, gathered)
        other = lax.ppermute(send, "mp", [(0, 1), (1, 0)])
        summed = keep.astype(jnp.float32) + other.astype(jnp.float32)
        return (current.astype(jnp.float32) + summed).astype(jnp.bfloat16)

    result = apply_layer(first)
    stored = jnp.where(segment_index == 0, result, jnp.zeros_like(result))

    for moment in range(1, segment_count):
        result = apply_layer(passed_along(result, "section"))
        stored = lax.optimization_barrier(jnp.where(segment_index == moment, result, stored))
    return stored.reshape(1, local_rows, width_local)


def solution(mesh):
    in_specs = (
        P("dp", "mp"),
        P("dp"),
        P("section", None),
        P("section", "dp", "mp"),
        P("section", "mp", "dp"),
    )
    out_specs = P("section", "dp", "mp")
    return jax.shard_map(
        per_device, mesh=mesh, in_specs=in_specs, out_specs=out_specs, check_vma=False
    )
```

```python
import jax
import jax.numpy as jnp
from jax import lax
from jax.experimental import pallas as pl
from jax.experimental.pallas import tpu as pltpu
from jax.sharding import PartitionSpec as P

TILE = 512


def ffn_body(own_ref, partner_ref, gain_ref, win_ref, wout_ref, keep_ref, send_ref, normed_ref, acc_ref):
    step = pl.program_id(0)
    half = keep_ref.shape[1]
    own = lax.axis_index("mp")
    own_cols = pl.ds(pl.multiple_of(own * half, 128), half)
    other_cols = pl.ds(pl.multiple_of((1 - own) * half, 128), half)

    @pl.when(step == 0)
    def _():
        mine = own_ref[...].astype(jnp.float32)
        theirs = partner_ref[...].astype(jnp.float32)
        total = jnp.sum(mine * mine, axis=-1, keepdims=True) + jnp.sum(
            theirs * theirs, axis=-1, keepdims=True
        )
        scale = lax.rsqrt(total / (2 * half) + 1e-06)
        normed_ref[:, own_cols] = (mine * scale * gain_ref[:, own_cols]).astype(normed_ref.dtype)
        normed_ref[:, other_cols] = (theirs * scale * gain_ref[:, other_cols]).astype(
            normed_ref.dtype
        )
        acc_ref[...] = jnp.zeros_like(acc_ref)

    pre = jnp.dot(normed_ref[...], win_ref[0], preferred_element_type=jnp.float32)
    hidden = (0.5 * pre * (1.0 + lax.erf(pre * 0.7071067811865476))).astype(jnp.bfloat16)
    acc_ref[...] += lax.dot_general(
        hidden, wout_ref[0], (((1,), (1,)), ((), ())), preferred_element_type=jnp.float32
    )

    @pl.when(step == pl.num_programs(0) - 1)
    def _():
        keep_ref[...] = acc_ref[:, own_cols].astype(keep_ref.dtype)
        send_ref[...] = acc_ref[:, other_cols].astype(send_ref.dtype)


def ffn(current, partner, gain, gathered):
    rows, half = current.shape
    width = 2 * half
    hidden_units = gathered.shape[2]
    return pl.pallas_call(
        ffn_body,
        grid=(hidden_units // TILE,),
        in_specs=[
            pl.BlockSpec((rows, half), lambda j: (0, 0)),
            pl.BlockSpec((rows, half), lambda j: (0, 0)),
            pl.BlockSpec((1, width), lambda j: (0, 0)),
            pl.BlockSpec((1, width, TILE), lambda j: (0, 0, j)),
            pl.BlockSpec((1, width, TILE), lambda j: (1, 0, j)),
        ],
        out_specs=[
            pl.BlockSpec((rows, half), lambda j: (0, 0)),
            pl.BlockSpec((rows, half), lambda j: (0, 0)),
        ],
        out_shape=[jax.ShapeDtypeStruct((rows, half), jnp.bfloat16)] * 2,
        scratch_shapes=[
            pltpu.VMEM((rows, width), jnp.bfloat16),
            pltpu.VMEM((rows, width), jnp.float32),
        ],
        compiler_params=pltpu.CompilerParams(vmem_limit_bytes=48 << 20),
    )(current, partner, gain, gathered, gathered)


RELAYED = 16


def shifted(value, axis, steps):
    count = lax.axis_size(axis)
    return lax.ppermute(value, axis, [(source, (source + steps) % count) for source in range(count)])


def passed_along(value, axis):
    count = lax.axis_size(axis)
    direct = shifted(value[:-RELAYED], axis, 1)
    relayed = value[-RELAYED:]
    for _ in range(count - 1):
        relayed = shifted(relayed, axis, -1)
    return jnp.concatenate([direct, relayed], axis=0)


def per_device(frames, frame_count, norm_gain, weight_in, weight_out):
    segment_count = lax.axis_size("section")
    segment_index = lax.axis_index("section")
    half_index = lax.axis_index("mp")
    both = jnp.stack([weight_in[0], weight_out[0].T])
    gathered = lax.all_gather(both, "dp", axis=1, tiled=True)
    local_rows, width_local = frames.shape
    live_count = frame_count[0]
    row_ids = jnp.arange(local_rows, dtype=jnp.int32)
    first = jnp.where((row_ids < live_count)[:, None], frames, jnp.zeros_like(frames))

    def apply_layer(current):
        partner = lax.ppermute(current, "mp", [(0, 1), (1, 0)])
        keep, send = ffn(current, partner, norm_gain, gathered)
        other = lax.ppermute(send, "mp", [(0, 1), (1, 0)])
        summed = keep.astype(jnp.float32) + other.astype(jnp.float32)
        return (current.astype(jnp.float32) + summed).astype(jnp.bfloat16)

    result = apply_layer(first)
    stored = jnp.where(segment_index == 0, result, jnp.zeros_like(result))

    for moment in range(1, segment_count):
        result = apply_layer(passed_along(result, "section"))
        stored = lax.optimization_barrier(jnp.where(segment_index == moment, result, stored))
    return stored.reshape(1, local_rows, width_local)


def solution(mesh):
    in_specs = (
        P("dp", "mp"),
        P("dp"),
        P("section", None),
        P("section", "dp", "mp"),
        P("section", "mp", "dp"),
    )
    out_specs = P("section", "dp", "mp")
    return jax.shard_map(
        per_device, mesh=mesh, in_specs=in_specs, out_specs=out_specs, check_vma=False
    )
```
